512 devices in a mesh: slab: 64 (over z, x, core), obs: 8 (over y).
Axes of the slice: x: 4, y: 8, z: 8, core: 2. Of those that a mesh axis runs over, the one named last changes fastest.
Arguments:
- background_members: float32 [64, 1048576], P('slab', 'obs'), may hold values from -6 to 6
- measurement_jitter: bfloat16 [64, 8, 65536], P(None, 'obs', 'slab'), may hold values from -5 to 5
- measurement_readings: float32 [8, 65536], P('obs', 'slab'), may hold values from -8 to 8
- measurement_noise_spread: float32 [8, 65536], P('obs', 'slab'), may hold values from 0.2 to 2
- measurement_grid_location: int32 [8, 65536], P('obs', 'slab'), may hold values from 0 to 2047
- active_tallies: int32 [8, 64], P('obs', 'slab'), may hold values from 128 to 1024, as said below
- coupling_listing: int32 [8, 2048, 8], P('obs', 'slab'), may hold values from 0 to 63, as said below
- taper_factors: float32 [8, 2048, 8], P('obs', 'slab'), may hold values from 0.1 to 1
Outputs:
- analysis: float32 [64, 1048576], P('slab', 'obs')
The draws below stay inside these ranges and needn't reach their ends.
Inputs may be any that keep to these rules, and one draw needn't show every extreme that they name: `active_tallies`: some region of some group holds 1024 live observations; slots beyond a region's count are padding. `coupling_listing`: the 8 observation blocks listed for a state block are distinct.
All inputs are finite; a program needn't handle non-finite values.
Results may differ from the reference program's by a relative error of at most 0.0063.
Values may be sent and summed in bfloat16 or wider, within the bound.
No kernel may reach another device: no remote copies, remote signals or barrier semaphores. Data moves between devices by JAX's collectives and lax.ppermute only.
A program may use at most 64 MiB of HBM per device.

```python
import math
import jax
import jax.numpy as jnp
from jax import lax

MEMBER_TOTAL = 64
BS = 64
OB = 128
L = 8
NBD = 32
OBD = 8
GROUPS = 8
REGIONS = 64
SP = 2048
OBSD = 1024
SLABBLK = 2048
SLABOBS = 65536
NOBG = 64
GRID_LOCATIONS = 1048576


def draw_active_tallies(key, part):
    key_low, key_full = jax.random.split(key)
    values = jax.random.randint(key_low, (GROUPS * REGIONS,), OBSD // 8, OBSD + 1, dtype=jnp.int32)
    fullest = jax.random.randint(key_full, (), 0, GROUPS * REGIONS, dtype=jnp.int32)
    values = jnp.where(jnp.arange(GROUPS * REGIONS, dtype=jnp.int32) == fullest, OBSD, values)
    return values.reshape(GROUPS, REGIONS)


def pick_blocks(row_key):
    return jax.random.permutation(row_key, NOBG)[:L]


def draw_coupling_listing(key, part):
    row_keys = jax.random.split(key, GROUPS * SLABBLK)
    chosen = jax.vmap(pick_blocks)(row_keys)
    return chosen.astype(jnp.int32).reshape(GROUPS, SLABBLK, L)


def place_ends(result, key, smallest, top_value):
    longest = result.shape.index(max(result.shape))
    spots = []
    for shift in (0, 1):
        where = [jax.random.randint(jax.random.fold_in(key, axis), (), 0, length) for axis, length in enumerate(result.shape)]
        where[longest] = (where[longest] + shift) % result.shape[longest]
        spots.append(tuple(where))
    return result.at[spots[0]].set(smallest).at[spots[1]].set(top_value)


def level_of(key, dims, cuts, smallest, largest):
    factor_of, own = 1.0, jax.random.fold_in(key, 6)
    for dim, shards_of in cuts:
        heights = jnp.exp(jax.random.uniform(jax.random.fold_in(own, dim), (shards_of,), jnp.float32, smallest / len(cuts), largest / len(cuts)))
        factor_of = factor_of * jnp.repeat(heights, dims[dim] // shards_of).reshape([-1 if axis == dim else 1 for axis in range(len(dims))])
    return factor_of


def scatter_about(key, extent, scale, limit, cuts=(), held_as=jnp.bfloat16):
    entries = jax.random.normal(key, extent, jnp.float32) * scale
    if len(cuts) > 0:
        entries = level_of(key, extent, cuts, -0.22, 0.18) * entries
    return jnp.clip(entries, min=-limit, max=limit).astype(held_as)


def setup_inputs(seed: int = 0) -> dict:
    seeds = jax.random.split(jax.random.key(seed), 9)
    background_members = scatter_about(seeds[0], (MEMBER_TOTAL, GRID_LOCATIONS), 1.0, 6.0, ((0, 64), (1, 8)), jnp.float32)
    measurement_jitter = scatter_about(seeds[1], (MEMBER_TOTAL, GROUPS, SLABOBS), 1.0, 5.0, ((1, 8), (2, 64)))
    measurement_readings = scatter_about(seeds[2], (GROUPS, SLABOBS), 2.0, 8.0, ((0, 8), (1, 64)), jnp.float32)
    measurement_noise_spread = jnp.clip(jnp.exp(math.log(2.0) - 2.3025851 * jax.random.uniform(seeds[3], (GROUPS, SLABOBS), jnp.float32) ** level_of(seeds[3], (GROUPS, SLABOBS), ((0, 8), (1, 64)), -0.2, 0.2)), 0.2, 2.0)
    measurement_grid_location = place_ends(jax.random.randint(seeds[4], (GROUPS, SLABOBS), 0, SP), jax.random.fold_in(seeds[4], 1), 0, SP - 1).astype(jnp.int32)
    active_tallies = draw_active_tallies(jax.random.fold_in(seeds[8], 71), 0)
    coupling_listing = draw_coupling_listing(jax.random.fold_in(seeds[8], 71), 0)
    taper_factors = jnp.clip(jnp.exp(math.log(1.0) - 2.3025851 * jax.random.uniform(seeds[7], (GROUPS, SLABBLK, L), jnp.float32) ** level_of(seeds[7], (GROUPS, SLABBLK, L), ((0, 8), (1, 64)), -0.2, 0.2)), 0.1, 1.0)
    return {"background_members": background_members, "measurement_jitter": measurement_jitter, "measurement_readings": measurement_readings, "measurement_noise_spread": measurement_noise_spread, "measurement_grid_location": measurement_grid_location, "active_tallies": active_tallies, "coupling_listing": coupling_listing, "taper_factors": taper_factors}


def reference(background_members, measurement_jitter, measurement_readings, measurement_noise_spread, measurement_grid_location, active_tallies, coupling_listing, taper_factors):
    highest = lax.Precision.HIGHEST
    temporary_storage = lax.optimization_barrier(background_members.astype(jnp.bfloat16)).astype(jnp.float32)
    state_tiles = temporary_storage.reshape(MEMBER_TOTAL, GROUPS, REGIONS, SP)
    deviation = state_tiles - jnp.mean(state_tiles, axis=0, keepdims=True)
    obs_places = jnp.broadcast_to(measurement_grid_location.reshape(1, GROUPS, REGIONS, OBSD), (MEMBER_TOTAL, GROUPS, REGIONS, OBSD))
    prior_value = jnp.take_along_axis(state_tiles, obs_places, axis=3)
    prior_shift = prior_value - jnp.mean(prior_value, axis=0, keepdims=True)
    spread = jnp.sum(prior_shift * prior_shift, axis=0, keepdims=True) / (MEMBER_TOTAL - 1)
    values = measurement_readings.reshape(1, GROUPS, REGIONS, OBSD)
    errors = measurement_noise_spread.reshape(1, GROUPS, REGIONS, OBSD)
    obs_noise = measurement_jitter.reshape(MEMBER_TOTAL, GROUPS, REGIONS, OBSD).astype(jnp.float32)
    usable = jnp.arange(OBSD, dtype=jnp.int32)[None, None, None, :] < active_tallies[None, :, :, None]
    innovation = (values + obs_noise - prior_value) / (spread + errors)
    gain_input = jnp.where(usable, innovation, jnp.float32(0.0))
    gain_low = lax.optimization_barrier(gain_input.astype(jnp.bfloat16)).astype(jnp.float32)
    prior_low = lax.optimization_barrier(prior_shift.astype(jnp.bfloat16)).astype(jnp.float32)

    def per_region(region):
        region_prior = lax.dynamic_index_in_dim(prior_low, region, 2, keepdims=False).reshape(MEMBER_TOTAL, GROUPS * OBD, OB)
        region_gain = lax.dynamic_index_in_dim(gain_low, region, 2, keepdims=False).reshape(MEMBER_TOTAL, GROUPS * OBD, OB)
        products = jnp.einsum("mco,nco->cmn", region_gain, region_prior, precision=highest)
        region_links = lax.dynamic_slice_in_dim(coupling_listing, region * NBD, NBD, 1)
        factor = lax.dynamic_slice_in_dim(taper_factors, region * NBD, NBD, 1) / (MEMBER_TOTAL - 1)
        choose = region_links[..., None] == jnp.arange(GROUPS * OBD, dtype=jnp.int32)
        localize = jnp.sum(jnp.where(choose, factor[..., None], jnp.float32(0.0)), axis=2)
        ensemble = jnp.einsum("gbc,cmn->gbmn", localize, products, precision=highest)
        region_dev = lax.dynamic_index_in_dim(deviation, region, 2, keepdims=False).reshape(MEMBER_TOTAL, GROUPS, NBD, BS)
        return jnp.einsum("gbmn,ngbp->mgbp", ensemble, region_dev, precision=highest)

    increments = lax.map(per_region, jnp.arange(REGIONS, dtype=jnp.int32))
    increments = jnp.moveaxis(increments, 0, 2).reshape(MEMBER_TOTAL, GRID_LOCATIONS)
    reduced_correction = lax.optimization_barrier(increments.astype(jnp.bfloat16)).astype(jnp.float32)
    return background_members + reduced_correction
```

```python
import jax
import jax.numpy as jnp
from jax import lax
from jax.sharding import PartitionSpec as P

OB = 128


highest = lax.Precision.HIGHEST


def block_products(
    tile_work,
    measurement_jitter,
    measurement_readings,
    measurement_noise_spread,
    measurement_grid_location,
    active_tallies,
):
    members = tile_work.shape[0]
    positions = measurement_grid_location[0]
    obs_count = positions.shape[0]
    prior_value = jnp.take(tile_work, positions, axis=1)
    prior_shift = prior_value - jnp.mean(prior_value, axis=0, keepdims=True)
    spread = jnp.sum(prior_shift * prior_shift, axis=0, keepdims=True) / (members - 1)
    usable = jnp.arange(obs_count, dtype=jnp.int32)[None, :] < active_tallies[0, 0]
    innovation = (
        measurement_readings + measurement_jitter[:, 0, :].astype(jnp.float32) - prior_value
    ) / (spread + measurement_noise_spread)
    gain_input = jnp.where(usable, innovation, jnp.float32(0.0)).astype(jnp.bfloat16)
    prior_low = prior_shift.astype(jnp.bfloat16)
    return jnp.einsum(
        "mco,nco->cmn",
        gain_input.reshape(members, -1, OB),
        prior_low.reshape(members, -1, OB),
        preferred_element_type=jnp.float32,
    )


def local(
    background_members,
    measurement_jitter,
    measurement_readings,
    measurement_noise_spread,
    measurement_grid_location,
    active_tallies,
    coupling_listing,
    taper_factors,
):
    work_low = background_members.astype(jnp.bfloat16)
    tile_low = lax.all_to_all(work_low, "slab", split_axis=1, concat_axis=0, tiled=True)
    tile_work = tile_low.astype(jnp.float32)
    members = tile_work.shape[0]
    blocks = coupling_listing.shape[1]
    deviation = tile_work - jnp.mean(tile_work, axis=0, keepdims=True)

    products = block_products(
        tile_work,
        measurement_jitter,
        measurement_readings,
        measurement_noise_spread,
        measurement_grid_location,
        active_tallies,
    )
    all_products = lax.all_gather(products, "obs", axis=0, tiled=True)
    obs_blocks = all_products.shape[0]

    block_links = coupling_listing[0]
    factor = taper_factors[0] / (members - 1)
    choose = block_links[..., None] == jnp.arange(obs_blocks, dtype=jnp.int32)
    localize = jnp.sum(jnp.where(choose, factor[..., None], jnp.float32(0.0)), axis=1)
    ensemble = jnp.einsum("bc,cmn->bmn", localize, all_products, precision=highest)
    region_dev = deviation.reshape(members, blocks, -1)
    increment = jnp.einsum("bmn,nbp->mbp", ensemble, region_dev, precision=highest)
    increment_low = increment.reshape(members, -1).astype(jnp.bfloat16)
    back = lax.all_to_all(increment_low, "slab", split_axis=0, concat_axis=1, tiled=True)
    return background_members + back.astype(jnp.float32)


def solution(mesh):
    return jax.shard_map(
        local,
        mesh=mesh,
        in_specs=(
            P("slab", "obs"),
            P(None, "obs", "slab"),
            P("obs", "slab"),
            P("obs", "slab"),
            P("obs", "slab"),
            P("obs", "slab"),
            P("obs", "slab", None),
            P("obs", "slab", None),
        ),
        out_specs=P("slab", "obs"),
        check_vma=False,
    )
```

```python
import jax
import jax.numpy as jnp
from jax import lax
from jax.sharding import PartitionSpec as P

OB = 128


highest = lax.Precision.HIGHEST


def block_products(
    tile_work,
    measurement_jitter,
    measurement_readings,
    measurement_noise_spread,
    measurement_grid_location,
    active_tallies,
):
    members = tile_work.shape[0]
    positions = measurement_grid_location[0]
    obs_count = positions.shape[0]
    prior_value = jnp.take(tile_work, positions, axis=1)
    prior_shift = prior_value - jnp.mean(prior_value, axis=0, keepdims=True)
    spread = jnp.sum(prior_shift * prior_shift, axis=0, keepdims=True) / (members - 1)
    usable = jnp.arange(obs_count, dtype=jnp.int32)[None, :] < active_tallies[0, 0]
    innovation = (
        measurement_readings + measurement_jitter[:, 0, :].astype(jnp.float32) - prior_value
    ) / (spread + measurement_noise_spread)
    gain_input = jnp.where(usable, innovation, jnp.float32(0.0)).astype(jnp.bfloat16)
    prior_low = prior_shift.astype(jnp.bfloat16)
    return jnp.einsum(
        "mco,nco->cmn",
        gain_input.reshape(members, -1, OB),
        prior_low.reshape(members, -1, OB),
        preferred_element_type=jnp.float32,
    )


def local(
    background_members,
    measurement_jitter,
    measurement_readings,
    measurement_noise_spread,
    measurement_grid_location,
    active_tallies,
    coupling_listing,
    taper_factors,
):
    work_low = background_members.astype(jnp.bfloat16)
    tile_low = lax.all_to_all(work_low, "slab", split_axis=1, concat_axis=0, tiled=True)
    tile_work = tile_low.astype(jnp.float32)
    members = tile_work.shape[0]
    blocks = coupling_listing.shape[1]
    deviation = tile_work - jnp.mean(tile_work, axis=0, keepdims=True)

    products = block_products(
        tile_work,
        measurement_jitter,
        measurement_readings,
        measurement_noise_spread,
        measurement_grid_location,
        active_tallies,
    )
    groups = lax.axis_size("obs")
    copies = jnp.broadcast_to(products[None], (groups,) + products.shape)
    all_products = lax.all_to_all(copies, "obs", split_axis=0, concat_axis=0, tiled=True)
    all_products = all_products.reshape((-1,) + products.shape[1:])
    obs_blocks = all_products.shape[0]

    block_links = coupling_listing[0]
    factor = taper_factors[0] / (members - 1)
    choose = block_links[..., None] == jnp.arange(obs_blocks, dtype=jnp.int32)
    localize = jnp.sum(jnp.where(choose, factor[..., None], jnp.float32(0.0)), axis=1)
    ensemble = jnp.einsum("bc,cmn->bmn", localize, all_products, precision=highest)
    region_dev = deviation.reshape(members, blocks, -1)
    increment = jnp.einsum("bmn,nbp->mbp", ensemble, region_dev, precision=highest)
    increment_low = increment.reshape(members, -1).astype(jnp.bfloat16)
    back = lax.all_to_all(increment_low, "slab", split_axis=0, concat_axis=1, tiled=True)
    return background_members + back.astype(jnp.float32)


def solution(mesh):
    return jax.shard_map(
        local,
        mesh=mesh,
        in_specs=(
            P("slab", "obs"),
            P(None, "obs", "slab"),
            P("obs", "slab"),
            P("obs", "slab"),
            P("obs", "slab"),
            P("obs", "slab"),
            P("obs", "slab", None),
            P("obs", "slab", None),
        ),
        out_specs=P("slab", "obs"),
        check_vma=False,
    )
```

```python
import jax
import jax.numpy as jnp
from jax import lax
from jax.sharding import PartitionSpec as P

OB = 128


highest = lax.Precision.HIGHEST


def block_products(
    tile_work,
    measurement_jitter,
    measurement_readings,
    measurement_noise_spread,
    measurement_grid_location,
    active_tallies,
):
    members = tile_work.shape[0]
    positions = measurement_grid_location[0]
    obs_count = positions.shape[0]
    prior_value = jnp.take(tile_work, positions, axis=1)
    prior_shift = prior_value - jnp.mean(prior_value, axis=0, keepdims=True)
    spread = jnp.sum(prior_shift * prior_shift, axis=0, keepdims=True) / (members - 1)
    usable = jnp.arange(obs_count, dtype=jnp.int32)[None, :] < active_tallies[0, 0]
    innovation = (
        measurement_readings + measurement_jitter[:, 0, :].astype(jnp.float32) - prior_value
    ) / (spread + measurement_noise_spread)
    gain_input = jnp.where(usable, innovation, jnp.float32(0.0)).astype(jnp.bfloat16)
    prior_low = prior_shift.astype(jnp.bfloat16)
    return jnp.einsum(
        "mco,nco->cmn",
        gain_input.reshape(members, -1, OB),
        prior_low.reshape(members, -1, OB),
        preferred_element_type=jnp.float32,
    )


def local(
    background_members,
    measurement_jitter,
    measurement_readings,
    measurement_noise_spread,
    measurement_grid_location,
    active_tallies,
    coupling_listing,
    taper_factors,
):
    members = lax.axis_size("slab")
    lanes = 128
    work_low = background_members.reshape(members, -1, lanes).astype(jnp.bfloat16)
    tile_low = lax.all_to_all(work_low, "slab", split_axis=0, concat_axis=0, tiled=True)
    tile_work = tile_low.reshape(members, -1).astype(jnp.float32)
    blocks = coupling_listing.shape[1]
    deviation = tile_work - jnp.mean(tile_work, axis=0, keepdims=True)

    products = block_products(
        tile_work,
        measurement_jitter,
        measurement_readings,
        measurement_noise_spread,
        measurement_grid_location,
        active_tallies,
    )
    groups = lax.axis_size("obs")
    flat = products.astype(jnp.bfloat16).reshape(products.shape[0], -1)
    copies = jnp.broadcast_to(flat[None], (groups,) + flat.shape)
    all_products = lax.all_to_all(copies, "obs", split_axis=0, concat_axis=0, tiled=True)
    all_products = all_products.reshape(-1, flat.shape[1]).astype(jnp.float32)
    obs_blocks = all_products.shape[0]

    block_links = coupling_listing[0]
    factor = taper_factors[0] / (members - 1)
    choose = block_links[..., None] == jnp.arange(obs_blocks, dtype=jnp.int32)
    localize = jnp.sum(jnp.where(choose, factor[..., None], jnp.float32(0.0)), axis=1)
    ensemble = jnp.dot(localize, all_products, precision=highest).reshape(blocks, members, members)
    region_dev = deviation.reshape(members, blocks, -1)
    increment = jnp.einsum("bmn,nbp->mbp", ensemble, region_dev, precision=highest)
    increment_low = increment.reshape(members, -1, lanes).astype(jnp.bfloat16)
    back = lax.all_to_all(increment_low, "slab", split_axis=0, concat_axis=0, tiled=True)
    return background_members + back.reshape(background_members.shape).astype(jnp.float32)


def solution(mesh):
    return jax.shard_map(
        local,
        mesh=mesh,
        in_specs=(
            P("slab", "obs"),
            P(None, "obs", "slab"),
            P("obs", "slab"),
            P("obs", "slab"),
            P("obs", "slab"),
            P("obs", "slab"),
            P("obs", "slab", None),
            P("obs", "slab", None),
        ),
        out_specs=P("slab", "obs"),
        check_vma=False,
    )
```

```python
import jax
import jax.numpy as jnp
from jax import lax
from jax.sharding import PartitionSpec as P

OB = 128


highest = lax.Precision.HIGHEST


def block_products(
    tile_work,
    measurement_jitter,
    measurement_readings,
    measurement_noise_spread,
    measurement_grid_location,
    active_tallies,
):
    members = tile_work.shape[0]
    positions = measurement_grid_location[0]
    obs_count = positions.shape[0]
    prior_value = jnp.take(tile_work, positions, axis=1)
    prior_shift = prior_value - jnp.mean(prior_value, axis=0, keepdims=True)
    spread = jnp.sum(prior_shift * prior_shift, axis=0, keepdims=True) / (members - 1)
    usable = jnp.arange(obs_count, dtype=jnp.int32)[None, :] < active_tallies[0, 0]
    innovation = (
        measurement_readings + measurement_jitter[:, 0, :].astype(jnp.float32) - prior_value
    ) / (spread + measurement_noise_spread)
    gain_input = jnp.where(usable, innovation, jnp.float32(0.0)).astype(jnp.bfloat16)
    prior_low = prior_shift.astype(jnp.bfloat16)
    return jnp.einsum(
        "mco,nco->cmn",
        gain_input.reshape(members, -1, OB),
        prior_low.reshape(members, -1, OB),
        preferred_element_type=jnp.float32,
    )


def local(
    background_members,
    measurement_jitter,
    measurement_readings,
    measurement_noise_spread,
    measurement_grid_location,
    active_tallies,
    coupling_listing,
    taper_factors,
):
    members = lax.axis_size("slab")
    lanes = 128
    pieces = background_members.reshape(members, -1, lanes)
    tile = lax.all_to_all(pieces, "slab", split_axis=0, concat_axis=0, tiled=True)
    tile_low = lax.optimization_barrier(tile.reshape(members, -1).astype(jnp.bfloat16))
    tile_work = tile_low.astype(jnp.float32)
    blocks = coupling_listing.shape[1]
    deviation = tile_work - jnp.mean(tile_work, axis=0, keepdims=True)

    products = block_products(
        tile_work,
        measurement_jitter,
        measurement_readings,
        measurement_noise_spread,
        measurement_grid_location,
        active_tallies,
    )
    groups = lax.axis_size("obs")
    flat = products.astype(jnp.bfloat16).reshape(products.shape[0], -1)
    copies = jnp.broadcast_to(flat[None], (groups,) + flat.shape)
    all_products = lax.all_to_all(copies, "obs", split_axis=0, concat_axis=0, tiled=True)
    all_products = all_products.reshape(-1, flat.shape[1]).astype(jnp.float32)
    obs_blocks = all_products.shape[0]

    block_links = coupling_listing[0]
    factor = taper_factors[0] / (members - 1)
    choose = block_links[..., None] == jnp.arange(obs_blocks, dtype=jnp.int32)
    localize = jnp.sum(jnp.where(choose, factor[..., None], jnp.float32(0.0)), axis=1)
    ensemble = jnp.dot(localize, all_products, precision=lax.Precision.HIGH)
    ensemble = ensemble.reshape(blocks, members, members)
    region_dev = deviation.reshape(members, blocks, -1)
    increment = jnp.einsum("bmn,nbp->mbp", ensemble, region_dev, precision=lax.Precision.HIGH)
    increment_low = increment.reshape(members, -1, lanes).astype(jnp.bfloat16)
    back = lax.all_to_all(increment_low, "slab", split_axis=0, concat_axis=0, tiled=True)
    return background_members + back.reshape(background_members.shape).astype(jnp.float32)


def solution(mesh):
    return jax.shard_map(
        local,
        mesh=mesh,
        in_specs=(
            P("slab", "obs"),
            P(None, "obs", "slab"),
            P("obs", "slab"),
            P("obs", "slab"),
            P("obs", "slab"),
            P("obs", "slab"),
            P("obs", "slab", None),
            P("obs", "slab", None),
        ),
        out_specs=P("slab", "obs"),
        check_vma=False,
    )
```

```python
import jax
import jax.numpy as jnp
from jax import lax
from jax.sharding import PartitionSpec as P

OB = 128


highest = lax.Precision.HIGHEST


def block_products(
    tile_low,
    observed,
    measurement_noise_spread,
    measurement_grid_location,
    active_tallies,
):
    members = tile_low.shape[0]
    positions = measurement_grid_location[0]
    obs_count = positions.shape[0]
    prior_value = jnp.take(tile_low, positions, axis=1).astype(jnp.float32)
    prior_shift = prior_value - jnp.mean(prior_value, axis=0, keepdims=True)
    spread = jnp.sum(prior_shift * prior_shift, axis=0, keepdims=True) / (members - 1)
    usable = jnp.arange(obs_count, dtype=jnp.int32)[None, :] < active_tallies[0, 0]
    innovation = (observed - prior_value) / (spread + measurement_noise_spread)
    gain_input = jnp.where(usable, innovation, jnp.float32(0.0)).astype(jnp.bfloat16)
    prior_low = prior_shift.astype(jnp.bfloat16)
    return jnp.einsum(
        "mco,nco->cmn",
        gain_input.reshape(members, -1, OB),
        prior_low.reshape(members, -1, OB),
        preferred_element_type=jnp.float32,
    )


def local(
    background_members,
    measurement_jitter,
    measurement_readings,
    measurement_noise_spread,
    measurement_grid_location,
    active_tallies,
    coupling_listing,
    taper_factors,
):
    members = lax.axis_size("slab")
    lanes = 128
    pieces = background_members.reshape(members, -1, lanes)
    tile = lax.all_to_all(pieces, "slab", split_axis=0, concat_axis=0, tiled=True)
    observed = measurement_readings + measurement_jitter[:, 0, :].astype(jnp.float32)
    tile_low, observed, noise = lax.optimization_barrier(
        (tile.reshape(members, -1).astype(jnp.bfloat16), observed, measurement_noise_spread)
    )
    tile_work = tile_low.astype(jnp.float32)
    blocks = coupling_listing.shape[1]
    deviation = tile_work - jnp.mean(tile_work, axis=0, keepdims=True)

    products = block_products(
        tile_low,
        observed,
        noise,
        measurement_grid_location,
        active_tallies,
    )
    groups = lax.axis_size("obs")
    flat = products.astype(jnp.bfloat16).reshape(products.shape[0], -1)
    copies = jnp.broadcast_to(flat[None], (groups,) + flat.shape)
    all_products = lax.all_to_all(copies, "obs", split_axis=0, concat_axis=0, tiled=True)
    all_products = all_products.reshape(-1, flat.shape[1]).astype(jnp.float32)
    obs_blocks = all_products.shape[0]

    block_links = coupling_listing[0]
    factor = taper_factors[0] / (members - 1)
    choose = block_links[..., None] == jnp.arange(obs_blocks, dtype=jnp.int32)
    localize = jnp.sum(jnp.where(choose, factor[..., None], jnp.float32(0.0)), axis=1)
    ensemble = jnp.dot(localize, all_products, precision=lax.Precision.HIGH)
    ensemble = ensemble.reshape(blocks, members, members)
    region_dev = deviation.reshape(members, blocks, -1)
    increment = jnp.einsum("bmn,nbp->mbp", ensemble, region_dev, precision=lax.Precision.HIGH)
    increment_low = increment.reshape(members, -1, lanes).astype(jnp.bfloat16)
    back = lax.all_to_all(increment_low, "slab", split_axis=0, concat_axis=0, tiled=True)
    return background_members + back.reshape(background_members.shape).astype(jnp.float32)


def solution(mesh):
    return jax.shard_map(
        local,
        mesh=mesh,
        in_specs=(
            P("slab", "obs"),
            P(None, "obs", "slab"),
            P("obs", "slab"),
            P("obs", "slab"),
            P("obs", "slab"),
            P("obs", "slab"),
            P("obs", "slab", None),
            P("obs", "slab", None),
        ),
        out_specs=P("slab", "obs"),
        check_vma=False,
    )
```

```python
import jax
import jax.numpy as jnp
from jax import lax
from jax.sharding import PartitionSpec as P

OB = 128


highest = lax.Precision.HIGHEST


def block_products(
    tile_work,
    observed,
    measurement_noise_spread,
    measurement_grid_location,
    active_tallies,
):
    members = tile_work.shape[0]
    positions = measurement_grid_location[0]
    obs_count = positions.shape[0]
    prior_value = jnp.take(tile_work, positions, axis=1)
    prior_shift = prior_value - jnp.mean(prior_value, axis=0, keepdims=True)
    spread = jnp.sum(prior_shift * prior_shift, axis=0, keepdims=True) / (members - 1)
    usable = jnp.arange(obs_count, dtype=jnp.int32)[None, :] < active_tallies[0, 0]
    innovation = (observed - prior_value) / (spread + measurement_noise_spread)
    gain_input = jnp.where(usable, innovation, jnp.float32(0.0)).astype(jnp.bfloat16)
    prior_low = prior_shift.astype(jnp.bfloat16)
    return jnp.einsum(
        "mco,nco->cmn",
        gain_input.reshape(members, -1, OB),
        prior_low.reshape(members, -1, OB),
        preferred_element_type=jnp.float32,
    )


def local(
    background_members,
    measurement_jitter,
    measurement_readings,
    measurement_noise_spread,
    measurement_grid_location,
    active_tallies,
    coupling_listing,
    taper_factors,
):
    members = lax.axis_size("slab")
    lanes = 128
    pieces = background_members.reshape(members, -1, lanes)
    tile = lax.all_to_all(pieces, "slab", split_axis=0, concat_axis=0, tiled=True)
    observed = measurement_readings + measurement_jitter[:, 0, :].astype(jnp.float32)
    tile_low, observed, noise = lax.optimization_barrier(
        (tile.reshape(members, -1).astype(jnp.bfloat16), observed, measurement_noise_spread)
    )
    tile_work = tile_low.astype(jnp.float32)
    blocks = coupling_listing.shape[1]
    deviation = tile_work - jnp.mean(tile_work, axis=0, keepdims=True)

    products = block_products(
        tile_work,
        observed,
        noise,
        measurement_grid_location,
        active_tallies,
    )
    groups = lax.axis_size("obs")
    flat = products.astype(jnp.bfloat16).reshape(products.shape[0], -1)
    copies = jnp.broadcast_to(flat[None], (groups,) + flat.shape)
    all_products = lax.all_to_all(copies, "obs", split_axis=0, concat_axis=0, tiled=True)
    all_products = all_products.reshape(-1, flat.shape[1]).astype(jnp.float32)
    obs_blocks = all_products.shape[0]

    block_links = coupling_listing[0]
    factor = taper_factors[0] / (members - 1)
    choose = block_links[..., None] == jnp.arange(obs_blocks, dtype=jnp.int32)
    localize = jnp.sum(jnp.where(choose, factor[..., None], jnp.float32(0.0)), axis=1)
    ensemble = jnp.dot(localize, all_products, precision=lax.Precision.HIGH)
    ensemble = ensemble.reshape(blocks, members, members)
    region_dev = deviation.reshape(members, blocks, -1)
    increment = jnp.einsum("bmn,nbp->mbp", ensemble, region_dev, precision=lax.Precision.HIGH)
    increment_low = increment.reshape(members, -1, lanes).astype(jnp.bfloat16)
    back = lax.all_to_all(increment_low, "slab", split_axis=0, concat_axis=0, tiled=True)
    return background_members + back.reshape(background_members.shape).astype(jnp.float32)


def solution(mesh):
    return jax.shard_map(
        local,
        mesh=mesh,
        in_specs=(
            P("slab", "obs"),
            P(None, "obs", "slab"),
            P("obs", "slab"),
            P("obs", "slab"),
            P("obs", "slab"),
            P("obs", "slab"),
            P("obs", "slab", None),
            P("obs", "slab", None),
        ),
        out_specs=P("slab", "obs"),
        check_vma=False,
    )
```

```python
import jax
import jax.numpy as jnp
from jax import lax
from jax.sharding import PartitionSpec as P

OB = 128


highest = lax.Precision.HIGHEST


def block_products(
    tile_low,
    tile_work,
    measurement_jitter,
    measurement_readings,
    measurement_noise_spread,
    measurement_grid_location,
    active_tallies,
):
    members = tile_work.shape[0]
    positions = measurement_grid_location[0]
    obs_count = positions.shape[0]
    points = tile_work.shape[1]
    pick = (jnp.arange(points, dtype=jnp.int32)[:, None] == positions[None, :]).astype(jnp.bfloat16)
    prior_value = jnp.dot(tile_low, pick, preferred_element_type=jnp.float32)
    prior_shift = prior_value - jnp.mean(prior_value, axis=0, keepdims=True)
    spread = jnp.sum(prior_shift * prior_shift, axis=0, keepdims=True) / (members - 1)
    usable = jnp.arange(obs_count, dtype=jnp.int32)[None, :] < active_tallies[0, 0]
    innovation = (
        measurement_readings + measurement_jitter[:, 0, :].astype(jnp.float32) - prior_value
    ) / (spread + measurement_noise_spread)
    gain_input = jnp.where(usable, innovation, jnp.float32(0.0)).astype(jnp.bfloat16)
    prior_low = prior_shift.astype(jnp.bfloat16)
    return jnp.einsum(
        "mco,nco->cmn",
        gain_input.reshape(members, -1, OB),
        prior_low.reshape(members, -1, OB),
        preferred_element_type=jnp.float32,
    )


def local(
    background_members,
    measurement_jitter,
    measurement_readings,
    measurement_noise_spread,
    measurement_grid_location,
    active_tallies,
    coupling_listing,
    taper_factors,
):
    members = lax.axis_size("slab")
    lanes = 128
    pieces = background_members.reshape(members, -1, lanes)
    tile = lax.all_to_all(pieces, "slab", split_axis=0, concat_axis=0, tiled=True)
    tile_low = lax.optimization_barrier(tile.reshape(members, -1).astype(jnp.bfloat16))
    tile_work = tile_low.astype(jnp.float32)
    blocks = coupling_listing.shape[1]
    deviation = tile_work - jnp.mean(tile_work, axis=0, keepdims=True)

    products = block_products(
        tile_low,
        tile_work,
        measurement_jitter,
        measurement_readings,
        measurement_noise_spread,
        measurement_grid_location,
        active_tallies,
    )
    groups = lax.axis_size("obs")
    flat = products.astype(jnp.bfloat16).reshape(products.shape[0], -1)
    copies = jnp.broadcast_to(flat[None], (groups,) + flat.shape)
    all_products = lax.all_to_all(copies, "obs", split_axis=0, concat_axis=0, tiled=True)
    all_products = all_products.reshape(-1, flat.shape[1]).astype(jnp.float32)
    obs_blocks = all_products.shape[0]

    block_links = coupling_listing[0]
    factor = taper_factors[0] / (members - 1)
    choose = block_links[..., None] == jnp.arange(obs_blocks, dtype=jnp.int32)
    localize = jnp.sum(jnp.where(choose, factor[..., None], jnp.float32(0.0)), axis=1)
    ensemble = jnp.dot(localize, all_products, precision=lax.Precision.HIGH)
    ensemble = ensemble.reshape(blocks, members, members)
    region_dev = deviation.reshape(members, blocks, -1)
    increment = jnp.einsum("bmn,nbp->mbp", ensemble, region_dev, precision=lax.Precision.HIGH)
    increment_low = increment.reshape(members, -1, lanes).astype(jnp.bfloat16)
    back = lax.all_to_all(increment_low, "slab", split_axis=0, concat_axis=0, tiled=True)
    return background_members + back.reshape(background_members.shape).astype(jnp.float32)


def solution(mesh):
    return jax.shard_map(
        local,
        mesh=mesh,
        in_specs=(
            P("slab", "obs"),
            P(None, "obs", "slab"),
            P("obs", "slab"),
            P("obs", "slab"),
            P("obs", "slab"),
            P("obs", "slab"),
            P("obs", "slab", None),
            P("obs", "slab", None),
        ),
        out_specs=P("slab", "obs"),
        check_vma=False,
    )
```

```python
import jax
import jax.numpy as jnp
from jax import lax
from jax.sharding import PartitionSpec as P

OB = 128


highest = lax.Precision.HIGHEST


def block_products(
    tile_low,
    tile_work,
    measurement_jitter,
    measurement_readings,
    measurement_noise_spread,
    measurement_grid_location,
    active_tallies,
):
    members = tile_work.shape[0]
    positions = measurement_grid_location[0]
    obs_count = positions.shape[0]
    points = tile_work.shape[1]
    pick = (jnp.arange(points, dtype=jnp.int32)[:, None] == positions[None, :]).astype(jnp.bfloat16)
    prior_value = jnp.dot(tile_low, pick, preferred_element_type=jnp.float32)
    prior_shift = prior_value - jnp.mean(prior_value, axis=0, keepdims=True)
    spread = jnp.sum(prior_shift * prior_shift, axis=0, keepdims=True) / (members - 1)
    usable = jnp.arange(obs_count, dtype=jnp.int32)[None, :] < active_tallies[0, 0]
    innovation = (
        measurement_readings + measurement_jitter[:, 0, :].astype(jnp.float32) - prior_value
    ) / (spread + measurement_noise_spread)
    gain_input = jnp.where(usable, innovation, jnp.float32(0.0)).astype(jnp.bfloat16)
    prior_low = prior_shift.astype(jnp.bfloat16)
    return jnp.einsum(
        "mco,nco->cmn",
        gain_input.reshape(members, -1, OB),
        prior_low.reshape(members, -1, OB),
        preferred_element_type=jnp.float32,
    )


def local(
    background_members,
    measurement_jitter,
    measurement_readings,
    measurement_noise_spread,
    measurement_grid_location,
    active_tallies,
    coupling_listing,
    taper_factors,
):
    members = lax.axis_size("slab")
    lanes = 128
    pieces = background_members.reshape(members, -1, lanes)
    tile = lax.all_to_all(pieces, "slab", split_axis=0, concat_axis=0, tiled=True)
    tile_low = lax.optimization_barrier(tile.reshape(members, -1).astype(jnp.bfloat16))
    tile_work = tile_low.astype(jnp.float32)
    blocks = coupling_listing.shape[1]
    deviation = tile_work - jnp.mean(tile_work, axis=0, keepdims=True)

    products = block_products(
        tile_low,
        tile_work,
        measurement_jitter,
        measurement_readings,
        measurement_noise_spread,
        measurement_grid_location,
        active_tallies,
    )
    groups = lax.axis_size("obs")
    flat = products.astype(jnp.bfloat16).reshape(products.shape[0], -1)
    copies = jnp.broadcast_to(flat[None], (groups,) + flat.shape)
    all_products = lax.all_to_all(copies, "obs", split_axis=0, concat_axis=0, tiled=True)
    all_products = all_products.reshape(-1, flat.shape[1])
    obs_blocks = all_products.shape[0]

    block_links = coupling_listing[0]
    factor = taper_factors[0] / (members - 1)
    choose = block_links[..., None] == jnp.arange(obs_blocks, dtype=jnp.int32)
    localize = jnp.sum(jnp.where(choose, factor[..., None], jnp.float32(0.0)), axis=1)
    localize_high = localize.astype(jnp.bfloat16)
    localize_low = (localize - localize_high.astype(jnp.float32)).astype(jnp.bfloat16)
    ensemble = jnp.dot(localize_high, all_products, preferred_element_type=jnp.float32) + jnp.dot(
        localize_low, all_products, preferred_element_type=jnp.float32
    )
    ensemble = ensemble.reshape(blocks, members, members)
    region_dev = deviation.reshape(members, blocks, -1)
    increment = jnp.einsum("bmn,nbp->mbp", ensemble, region_dev, precision=lax.Precision.HIGH)
    increment_low = increment.reshape(members, -1, lanes).astype(jnp.bfloat16)
    back = lax.all_to_all(increment_low, "slab", split_axis=0, concat_axis=0, tiled=True)
    return background_members + back.reshape(background_members.shape).astype(jnp.float32)


def solution(mesh):
    return jax.shard_map(
        local,
        mesh=mesh,
        in_specs=(
            P("slab", "obs"),
            P(None, "obs", "slab"),
            P("obs", "slab"),
            P("obs", "slab"),
            P("obs", "slab"),
            P("obs", "slab"),
            P("obs", "slab", None),
            P("obs", "slab", None),
        ),
        out_specs=P("slab", "obs"),
        check_vma=False,
    )
```

```python
import jax
import jax.numpy as jnp
from jax import lax
from jax.sharding import PartitionSpec as P

OB = 128


highest = lax.Precision.HIGHEST


def block_products(
    tile_low,
    tile_work,
    measurement_jitter,
    measurement_readings,
    measurement_noise_spread,
    measurement_grid_location,
    active_tallies,
):
    members = tile_work.shape[0]
    positions = measurement_grid_location[0]
    obs_count = positions.shape[0]
    points = tile_work.shape[1]
    pick = (jnp.arange(points, dtype=jnp.int32)[:, None] == positions[None, :]).astype(jnp.bfloat16)
    prior_value = jnp.dot(tile_low, pick, preferred_element_type=jnp.float32)
    prior_shift = prior_value - jnp.mean(prior_value, axis=0, keepdims=True)
    spread = jnp.sum(prior_shift * prior_shift, axis=0, keepdims=True) / (members - 1)
    usable = jnp.arange(obs_count, dtype=jnp.int32)[None, :] < active_tallies[0, 0]
    innovation = (
        measurement_readings + measurement_jitter[:, 0, :].astype(jnp.float32) - prior_value
    ) / (spread + measurement_noise_spread)
    gain_input = jnp.where(usable, innovation, jnp.float32(0.0)).astype(jnp.bfloat16)
    prior_low = prior_shift.astype(jnp.bfloat16)
    return jnp.einsum(
        "mco,nco->cmn",
        gain_input.reshape(members, -1, OB),
        prior_low.reshape(members, -1, OB),
        preferred_element_type=jnp.float32,
    )


def local(
    background_members,
    measurement_jitter,
    measurement_readings,
    measurement_noise_spread,
    measurement_grid_location,
    active_tallies,
    coupling_listing,
    taper_factors,
):
    members = lax.axis_size("slab")
    lanes = 128
    pieces = background_members.reshape(members, -1, lanes)
    tile = lax.all_to_all(pieces, "slab", split_axis=0, concat_axis=0, tiled=True)
    tile_low = lax.optimization_barrier(tile.reshape(members, -1).astype(jnp.bfloat16))
    tile_work = tile_low.astype(jnp.float32)
    blocks = coupling_listing.shape[1]
    deviation = tile_work - jnp.mean(tile_work, axis=0, keepdims=True)

    products = block_products(
        tile_low,
        tile_work,
        measurement_jitter,
        measurement_readings,
        measurement_noise_spread,
        measurement_grid_location,
        active_tallies,
    )
    groups = lax.axis_size("obs")
    flat = products.astype(jnp.bfloat16).reshape(products.shape[0], -1)
    copies = jnp.broadcast_to(flat[None], (groups,) + flat.shape)
    all_products = lax.all_to_all(copies, "obs", split_axis=0, concat_axis=0, tiled=True)
    all_products = all_products.reshape(-1, flat.shape[1])
    obs_blocks = all_products.shape[0]

    block_links = coupling_listing[0]
    factor = taper_factors[0] / (members - 1)
    choose = block_links[..., None] == jnp.arange(obs_blocks, dtype=jnp.int32)
    localize = jnp.sum(jnp.where(choose, factor[..., None], jnp.float32(0.0)), axis=1)
    localize_high = lax.optimization_barrier(localize.astype(jnp.bfloat16))
    localize_low = (localize - localize_high.astype(jnp.float32)).astype(jnp.bfloat16)
    ensemble = jnp.dot(localize_high, all_products, preferred_element_type=jnp.float32) + jnp.dot(
        localize_low, all_products, preferred_element_type=jnp.float32
    )
    ensemble = ensemble.reshape(blocks, members, members)
    region_dev = deviation.reshape(members, blocks, -1)
    increment = jnp.einsum("bmn,nbp->mbp", ensemble, region_dev, precision=lax.Precision.HIGH)
    increment_low = increment.reshape(members, -1, lanes).astype(jnp.bfloat16)
    back = lax.all_to_all(increment_low, "slab", split_axis=0, concat_axis=0, tiled=True)
    return background_members + back.reshape(background_members.shape).astype(jnp.float32)


def solution(mesh):
    return jax.shard_map(
        local,
        mesh=mesh,
        in_specs=(
            P("slab", "obs"),
            P(None, "obs", "slab"),
            P("obs", "slab"),
            P("obs", "slab"),
            P("obs", "slab"),
            P("obs", "slab"),
            P("obs", "slab", None),
            P("obs", "slab", None),
        ),
        out_specs=P("slab", "obs"),
        check_vma=False,
    )
```

```python
import jax
import jax.numpy as jnp
from jax import lax
from jax.sharding import PartitionSpec as P

OB = 128


highest = lax.Precision.HIGHEST


def block_products(
    tile_low,
    tile_work,
    measurement_jitter,
    measurement_readings,
    measurement_noise_spread,
    measurement_grid_location,
    active_tallies,
):
    members = tile_work.shape[0]
    positions = measurement_grid_location[0]
    obs_count = positions.shape[0]
    points = tile_work.shape[1]
    pick = (jnp.arange(points, dtype=jnp.int32)[:, None] == positions[None, :]).astype(jnp.bfloat16)
    prior_value = jnp.dot(tile_low, pick, preferred_element_type=jnp.float32)
    prior_shift = prior_value - jnp.mean(prior_value, axis=0, keepdims=True)
    spread = jnp.sum(prior_shift * prior_shift, axis=0, keepdims=True) / (members - 1)
    usable = jnp.arange(obs_count, dtype=jnp.int32)[None, :] < active_tallies[0, 0]
    innovation = (
        measurement_readings + measurement_jitter[:, 0, :].astype(jnp.float32) - prior_value
    ) / (spread + measurement_noise_spread)
    gain_input = jnp.where(usable, innovation, jnp.float32(0.0)).astype(jnp.bfloat16)
    prior_low = prior_shift.astype(jnp.bfloat16)
    return jnp.einsum(
        "mco,nco->cmn",
        gain_input.reshape(members, -1, OB),
        prior_low.reshape(members, -1, OB),
        preferred_element_type=jnp.float32,
    )


def local(
    background_members,
    measurement_jitter,
    measurement_readings,
    measurement_noise_spread,
    measurement_grid_location,
    active_tallies,
    coupling_listing,
    taper_factors,
):
    members = lax.axis_size("slab")
    lanes = 128
    pieces = background_members.reshape(members, -1, lanes)
    tile = lax.all_to_all(pieces, "slab", split_axis=0, concat_axis=0, tiled=True)
    tile_work = lax.reduce_precision(tile.reshape(members, -1), exponent_bits=8, mantissa_bits=7)
    tile_work = lax.optimization_barrier(tile_work)
    tile_low = tile_work.astype(jnp.bfloat16)
    blocks = coupling_listing.shape[1]
    deviation = tile_work - jnp.mean(tile_work, axis=0, keepdims=True)

    products = block_products(
        tile_low,
        tile_work,
        measurement_jitter,
        measurement_readings,
        measurement_noise_spread,
        measurement_grid_location,
        active_tallies,
    )
    groups = lax.axis_size("obs")
    flat = products.astype(jnp.bfloat16).reshape(products.shape[0], -1)
    copies = jnp.broadcast_to(flat[None], (groups,) + flat.shape)
    all_products = lax.all_to_all(copies, "obs", split_axis=0, concat_axis=0, tiled=True)
    all_products = all_products.reshape(-1, flat.shape[1])
    obs_blocks = all_products.shape[0]

    block_links = coupling_listing[0]
    factor = taper_factors[0] / (members - 1)
    choose = block_links[..., None] == jnp.arange(obs_blocks, dtype=jnp.int32)
    localize = jnp.sum(jnp.where(choose, factor[..., None], jnp.float32(0.0)), axis=1)
    localize_high = lax.optimization_barrier(localize.astype(jnp.bfloat16))
    localize_low = (localize - localize_high.astype(jnp.float32)).astype(jnp.bfloat16)
    ensemble = jnp.dot(localize_high, all_products, preferred_element_type=jnp.float32) + jnp.dot(
        localize_low, all_products, preferred_element_type=jnp.float32
    )
    ensemble = ensemble.reshape(blocks, members, members)
    region_dev = deviation.reshape(members, blocks, -1)
    increment = jnp.einsum("bmn,nbp->mbp", ensemble, region_dev, precision=lax.Precision.HIGH)
    increment_low = increment.reshape(members, -1, lanes).astype(jnp.bfloat16)
    back = lax.all_to_all(increment_low, "slab", split_axis=0, concat_axis=0, tiled=True)
    return background_members + back.reshape(background_members.shape).astype(jnp.float32)


def solution(mesh):
    return jax.shard_map(
        local,
        mesh=mesh,
        in_specs=(
            P("slab", "obs"),
            P(None, "obs", "slab"),
            P("obs", "slab"),
            P("obs", "slab"),
            P("obs", "slab"),
            P("obs", "slab"),
            P("obs", "slab", None),
            P("obs", "slab", None),
        ),
        out_specs=P("slab", "obs"),
        check_vma=False,
    )
```

```python
import jax
import jax.numpy as jnp
from jax import lax
from jax.sharding import PartitionSpec as P

OB = 128


highest = lax.Precision.HIGHEST


def block_products(
    tile_low,
    tile_work,
    measurement_jitter,
    measurement_readings,
    measurement_noise_spread,
    measurement_grid_location,
    active_tallies,
):
    members = tile_work.shape[0]
    positions = measurement_grid_location[0]
    obs_count = positions.shape[0]
    points = tile_work.shape[1]
    pick = (jnp.arange(points, dtype=jnp.int32)[:, None] == positions[None, :]).astype(jnp.bfloat16)
    prior_value = jnp.dot(tile_low, pick, preferred_element_type=jnp.float32)
    prior_shift = prior_value - jnp.mean(prior_value, axis=0, keepdims=True)
    spread = jnp.sum(prior_shift * prior_shift, axis=0, keepdims=True) / (members - 1)
    usable = jnp.arange(obs_count, dtype=jnp.int32)[None, :] < active_tallies[0, 0]
    innovation = (
        measurement_readings + measurement_jitter[:, 0, :].astype(jnp.float32) - prior_value
    ) / (spread + measurement_noise_spread)
    gain_input = jnp.where(usable, innovation, jnp.float32(0.0)).astype(jnp.bfloat16)
    prior_low = prior_shift.astype(jnp.bfloat16)
    return jnp.einsum(
        "mco,nco->cmn",
        gain_input.reshape(members, -1, OB),
        prior_low.reshape(members, -1, OB),
        preferred_element_type=jnp.float32,
    )


def local(
    background_members,
    measurement_jitter,
    measurement_readings,
    measurement_noise_spread,
    measurement_grid_location,
    active_tallies,
    coupling_listing,
    taper_factors,
):
    members = lax.axis_size("slab")
    lanes = 128
    pieces = background_members.reshape(members, -1, lanes)
    tile = lax.all_to_all(pieces, "slab", split_axis=0, concat_axis=0, tiled=True)
    tile_low = lax.optimization_barrier(tile.reshape(members, -1).astype(jnp.bfloat16))
    tile_work = tile_low.astype(jnp.float32)
    blocks = coupling_listing.shape[1]
    deviation = tile_work - jnp.mean(tile_work, axis=0, keepdims=True)

    products = block_products(
        tile_low,
        tile_work,
        measurement_jitter,
        measurement_readings,
        measurement_noise_spread,
        measurement_grid_location,
        active_tallies,
    )
    groups = lax.axis_size("obs")
    flat = products.astype(jnp.bfloat16).reshape(products.shape[0], -1)
    copies = jnp.broadcast_to(flat[None], (groups,) + flat.shape)
    all_products = lax.all_to_all(copies, "obs", split_axis=0, concat_axis=0, tiled=True)
    all_products = all_products.reshape(-1, flat.shape[1])
    obs_blocks = all_products.shape[0]

    block_links = coupling_listing[0]
    factor = taper_factors[0] / (members - 1)
    choose = block_links[..., None] == jnp.arange(obs_blocks, dtype=jnp.int32)
    localize = jnp.sum(jnp.where(choose, factor[..., None], jnp.float32(0.0)), axis=1)
    localize_high = lax.optimization_barrier(localize.astype(jnp.bfloat16))
    localize_low = (localize - localize_high.astype(jnp.float32)).astype(jnp.bfloat16)
    ensemble = jnp.dot(localize_high, all_products, preferred_element_type=jnp.float32) + jnp.dot(
        localize_low, all_products, preferred_element_type=jnp.float32
    )
    ensemble = ensemble.reshape(blocks, members, members)
    region_dev = deviation.reshape(members, blocks, -1)
    increment = jnp.einsum("bmn,nbp->mbp", ensemble, region_dev, precision=lax.Precision.HIGH)
    increment_low = increment.reshape(members, -1, lanes).astype(jnp.bfloat16)
    back = lax.all_to_all(increment_low, "slab", split_axis=0, concat_axis=0, tiled=True)
    analysis = pieces + back.astype(jnp.float32)
    return analysis.reshape(background_members.shape)


def solution(mesh):
    return jax.shard_map(
        local,
        mesh=mesh,
        in_specs=(
            P("slab", "obs"),
            P(None, "obs", "slab"),
            P("obs", "slab"),
            P("obs", "slab"),
            P("obs", "slab"),
            P("obs", "slab"),
            P("obs", "slab", None),
            P("obs", "slab", None),
        ),
        out_specs=P("slab", "obs"),
        check_vma=False,
    )
```

```python
import jax
import jax.numpy as jnp
from jax import lax
from jax.sharding import PartitionSpec as P

OB = 128


highest = lax.Precision.HIGHEST


def block_products(
    tile_low,
    tile_work,
    measurement_jitter,
    measurement_readings,
    measurement_noise_spread,
    measurement_grid_location,
    active_tallies,
):
    members = tile_work.shape[0]
    positions = measurement_grid_location[0]
    obs_count = positions.shape[0]
    points = tile_work.shape[1]
    pick = (jnp.arange(points, dtype=jnp.int32)[:, None] == positions[None, :]).astype(jnp.bfloat16)
    prior_value = jnp.dot(tile_low, pick, preferred_element_type=jnp.float32)
    prior_shift = prior_value - jnp.mean(prior_value, axis=0, keepdims=True)
    spread = jnp.sum(prior_shift * prior_shift, axis=0, keepdims=True) / (members - 1)
    usable = jnp.arange(obs_count, dtype=jnp.int32)[None, :] < active_tallies[0, 0]
    innovation = (
        measurement_readings + measurement_jitter[:, 0, :].astype(jnp.float32) - prior_value
    ) / (spread + measurement_noise_spread)
    gain_input = jnp.where(usable, innovation, jnp.float32(0.0)).astype(jnp.bfloat16)
    prior_low = prior_shift.astype(jnp.bfloat16)
    return jnp.einsum(
        "mco,nco->cmn",
        gain_input.reshape(members, -1, OB),
        prior_low.reshape(members, -1, OB),
        preferred_element_type=jnp.float32,
    )


def local(
    background_members,
    measurement_jitter,
    measurement_readings,
    measurement_noise_spread,
    measurement_grid_location,
    active_tallies,
    coupling_listing,
    taper_factors,
):
    members = lax.axis_size("slab")
    lanes = 128
    pieces = background_members.reshape(members, -1, lanes)
    tile = lax.all_to_all(pieces, "slab", split_axis=0, concat_axis=0, tiled=True)
    tile_low = lax.optimization_barrier(tile.reshape(members, -1).astype(jnp.bfloat16))
    tile_work = tile_low.astype(jnp.float32)
    blocks = coupling_listing.shape[1]
    deviation = tile_work - jnp.mean(tile_work, axis=0, keepdims=True)

    products = block_products(
        tile_low,
        tile_work,
        measurement_jitter,
        measurement_readings,
        measurement_noise_spread,
        measurement_grid_location,
        active_tallies,
    )
    groups = lax.axis_size("obs")
    block_size = products.shape[1] * products.shape[2]
    flat = products.astype(jnp.bfloat16).reshape(16, -1)
    copies = jnp.broadcast_to(flat[None], (groups,) + flat.shape)
    all_products = lax.all_to_all(copies, "obs", split_axis=0, concat_axis=0, tiled=True)
    all_products = all_products.reshape(-1, block_size)
    obs_blocks = all_products.shape[0]

    block_links = coupling_listing[0]
    factor = taper_factors[0] / (members - 1)
    choose = block_links[..., None] == jnp.arange(obs_blocks, dtype=jnp.int32)
    localize = jnp.sum(jnp.where(choose, factor[..., None], jnp.float32(0.0)), axis=1)
    localize_high = lax.optimization_barrier(localize.astype(jnp.bfloat16))
    localize_low = (localize - localize_high.astype(jnp.float32)).astype(jnp.bfloat16)
    ensemble = jnp.dot(localize_high, all_products, preferred_element_type=jnp.float32) + jnp.dot(
        localize_low, all_products, preferred_element_type=jnp.float32
    )
    ensemble = ensemble.reshape(blocks, members, members)
    region_dev = deviation.reshape(members, blocks, -1)
    increment = jnp.einsum("bmn,nbp->mbp", ensemble, region_dev, precision=lax.Precision.HIGH)
    increment_low = increment.reshape(members, -1, lanes).astype(jnp.bfloat16)
    back = lax.all_to_all(increment_low, "slab", split_axis=0, concat_axis=0, tiled=True)
    analysis = pieces + back.astype(jnp.float32)
    return analysis.reshape(background_members.shape)


def solution(mesh):
    return jax.shard_map(
        local,
        mesh=mesh,
        in_specs=(
            P("slab", "obs"),
            P(None, "obs", "slab"),
            P("obs", "slab"),
            P("obs", "slab"),
            P("obs", "slab"),
            P("obs", "slab"),
            P("obs", "slab", None),
            P("obs", "slab", None),
        ),
        out_specs=P("slab", "obs"),
        check_vma=False,
    )
```

```python
import jax
import jax.numpy as jnp
from jax import lax
from jax.sharding import PartitionSpec as P

OB = 128


highest = lax.Precision.HIGHEST


def block_products(
    tile_low,
    tile_work,
    measurement_jitter,
    measurement_readings,
    measurement_noise_spread,
    measurement_grid_location,
    active_tallies,
):
    members = tile_work.shape[0]
    positions = measurement_grid_location[0]
    obs_count = positions.shape[0]
    points = tile_work.shape[1]
    pick = (jnp.arange(points, dtype=jnp.int32)[:, None] == positions[None, :]).astype(jnp.bfloat16)
    prior_value = jnp.dot(tile_low, pick, preferred_element_type=jnp.float32)
    prior_shift = prior_value - jnp.mean(prior_value, axis=0, keepdims=True)
    spread = jnp.sum(prior_shift * prior_shift, axis=0, keepdims=True) / (members - 1)
    usable = jnp.arange(obs_count, dtype=jnp.int32)[None, :] < active_tallies[0, 0]
    innovation = (
        measurement_readings + measurement_jitter[:, 0, :].astype(jnp.float32) - prior_value
    ) / (spread + measurement_noise_spread)
    gain_input = jnp.where(usable, innovation, jnp.float32(0.0)).astype(jnp.bfloat16)
    prior_low = prior_shift.astype(jnp.bfloat16)
    return jnp.einsum(
        "mco,nco->cmn",
        gain_input.reshape(members, -1, OB),
        prior_low.reshape(members, -1, OB),
        preferred_element_type=jnp.float32,
    )


def local(
    background_members,
    measurement_jitter,
    measurement_readings,
    measurement_noise_spread,
    measurement_grid_location,
    active_tallies,
    coupling_listing,
    taper_factors,
):
    members = lax.axis_size("slab")
    lanes = 128
    pieces = background_members.reshape(members, -1, lanes)
    tile = lax.all_to_all(pieces, "slab", split_axis=0, concat_axis=0, tiled=True)
    tile_low = lax.optimization_barrier(tile.reshape(members, -1).astype(jnp.bfloat16))
    tile_work = tile_low.astype(jnp.float32)
    blocks = coupling_listing.shape[1]

    products = block_products(
        tile_low,
        tile_work,
        measurement_jitter,
        measurement_readings,
        measurement_noise_spread,
        measurement_grid_location,
        active_tallies,
    )
    groups = lax.axis_size("obs")
    flat = products.astype(jnp.bfloat16).reshape(products.shape[0], -1)
    copies = jnp.broadcast_to(flat[None], (groups,) + flat.shape)
    all_products = lax.all_to_all(copies, "obs", split_axis=0, concat_axis=0, tiled=True)
    all_products = all_products.reshape(-1, flat.shape[1])
    obs_blocks = all_products.shape[0]

    block_links = coupling_listing[0]
    factor = taper_factors[0] / (members - 1)
    choose = block_links[..., None] == jnp.arange(obs_blocks, dtype=jnp.int32)
    localize = jnp.sum(jnp.where(choose, factor[..., None], jnp.float32(0.0)), axis=1)
    localize_high = lax.optimization_barrier(localize.astype(jnp.bfloat16))
    localize_low = (localize - localize_high.astype(jnp.float32)).astype(jnp.bfloat16)
    ensemble = jnp.dot(localize_high, all_products, preferred_element_type=jnp.float32) + jnp.dot(
        localize_low, all_products, preferred_element_type=jnp.float32
    )
    ensemble = ensemble.reshape(blocks, members, members)
    region_work = tile_low.reshape(members, blocks, -1)
    ensemble_high = lax.optimization_barrier(ensemble.astype(jnp.bfloat16))
    ensemble_low = (ensemble - ensemble_high.astype(jnp.float32)).astype(jnp.bfloat16)
    increment = jnp.einsum(
        "bmn,nbp->mbp", ensemble_high, region_work, preferred_element_type=jnp.float32
    ) + jnp.einsum("bmn,nbp->mbp", ensemble_low, region_work, preferred_element_type=jnp.float32)
    region_mean = jnp.mean(tile_work, axis=0).reshape(blocks, -1)
    increment = increment - jnp.sum(ensemble, axis=2).T[:, :, None] * region_mean[None]
    increment_low = increment.reshape(members, -1, lanes).astype(jnp.bfloat16)
    back = lax.all_to_all(increment_low, "slab", split_axis=0, concat_axis=0, tiled=True)
    analysis = pieces + back.astype(jnp.float32)
    return analysis.reshape(background_members.shape)


def solution(mesh):
    return jax.shard_map(
        local,
        mesh=mesh,
        in_specs=(
            P("slab", "obs"),
            P(None, "obs", "slab"),
            P("obs", "slab"),
            P("obs", "slab"),
            P("obs", "slab"),
            P("obs", "slab"),
            P("obs", "slab", None),
            P("obs", "slab", None),
        ),
        out_specs=P("slab", "obs"),
        check_vma=False,
    )
```

```python
import jax
import jax.numpy as jnp
from jax import lax
from jax.sharding import PartitionSpec as P

OB = 128


highest = lax.Precision.HIGHEST


def block_products(
    tile_low,
    tile_work,
    measurement_jitter,
    measurement_readings,
    measurement_noise_spread,
    measurement_grid_location,
    active_tallies,
):
    members = tile_work.shape[0]
    positions = measurement_grid_location[0]
    obs_count = positions.shape[0]
    points = tile_work.shape[1]
    pick = (positions[:, None] == jnp.arange(points, dtype=jnp.int32)[None, :]).astype(jnp.bfloat16)
    prior_value = jnp.einsum("kq,mq->mk", pick, tile_low, preferred_element_type=jnp.float32)
    prior_shift = prior_value - jnp.mean(prior_value, axis=0, keepdims=True)
    spread = jnp.sum(prior_shift * prior_shift, axis=0, keepdims=True) / (members - 1)
    usable = jnp.arange(obs_count, dtype=jnp.int32)[None, :] < active_tallies[0, 0]
    innovation = (
        measurement_readings + measurement_jitter[:, 0, :].astype(jnp.float32) - prior_value
    ) / (spread + measurement_noise_spread)
    gain_input = jnp.where(usable, innovation, jnp.float32(0.0)).astype(jnp.bfloat16)
    prior_low = prior_shift.astype(jnp.bfloat16)
    return jnp.einsum(
        "mco,nco->cmn",
        gain_input.reshape(members, -1, OB),
        prior_low.reshape(members, -1, OB),
        preferred_element_type=jnp.float32,
    )


def local(
    background_members,
    measurement_jitter,
    measurement_readings,
    measurement_noise_spread,
    measurement_grid_location,
    active_tallies,
    coupling_listing,
    taper_factors,
):
    members = lax.axis_size("slab")
    lanes = 128
    pieces = background_members.reshape(members, -1, lanes)
    tile = lax.all_to_all(pieces, "slab", split_axis=0, concat_axis=0, tiled=True)
    tile_low = lax.optimization_barrier(tile.reshape(members, -1).astype(jnp.bfloat16))
    tile_work = tile_low.astype(jnp.float32)
    blocks = coupling_listing.shape[1]
    deviation = tile_work - jnp.mean(tile_work, axis=0, keepdims=True)

    products = block_products(
        tile_low,
        tile_work,
        measurement_jitter,
        measurement_readings,
        measurement_noise_spread,
        measurement_grid_location,
        active_tallies,
    )
    groups = lax.axis_size("obs")
    flat = products.astype(jnp.bfloat16).reshape(products.shape[0], -1)
    copies = jnp.broadcast_to(flat[None], (groups,) + flat.shape)
    all_products = lax.all_to_all(copies, "obs", split_axis=0, concat_axis=0, tiled=True)
    all_products = all_products.reshape(-1, flat.shape[1])
    obs_blocks = all_products.shape[0]

    block_links = coupling_listing[0]
    factor = taper_factors[0] / (members - 1)
    choose = block_links[..., None] == jnp.arange(obs_blocks, dtype=jnp.int32)
    localize = jnp.sum(jnp.where(choose, factor[..., None], jnp.float32(0.0)), axis=1)
    localize_high = lax.optimization_barrier(localize.astype(jnp.bfloat16))
    localize_low = (localize - localize_high.astype(jnp.float32)).astype(jnp.bfloat16)
    ensemble = jnp.dot(localize_high, all_products, preferred_element_type=jnp.float32) + jnp.dot(
        localize_low, all_products, preferred_element_type=jnp.float32
    )
    ensemble = ensemble.reshape(blocks, members, members)
    region_dev = deviation.reshape(members, blocks, -1)
    increment = jnp.einsum("bmn,nbp->mbp", ensemble, region_dev, precision=lax.Precision.HIGH)
    increment_low = increment.reshape(members, -1, lanes).astype(jnp.bfloat16)
    back = lax.all_to_all(increment_low, "slab", split_axis=0, concat_axis=0, tiled=True)
    analysis = pieces + back.astype(jnp.float32)
    return analysis.reshape(background_members.shape)


def solution(mesh):
    return jax.shard_map(
        local,
        mesh=mesh,
        in_specs=(
            P("slab", "obs"),
            P(None, "obs", "slab"),
            P("obs", "slab"),
            P("obs", "slab"),
            P("obs", "slab"),
            P("obs", "slab"),
            P("obs", "slab", None),
            P("obs", "slab", None),
        ),
        out_specs=P("slab", "obs"),
        check_vma=False,
    )
```
